512 devices in a mesh: gx: 16 (over z), gy: 8 (over y, x_lo), gz: 4 (over x_hi, core).
Axes of the slice: x: 4 (x_hi: 2, x_lo: 2; x = x_hi * 2 + x_lo), y: 4, z: 16, core: 2. Of those that a mesh axis runs over, the one named last changes fastest.
Arguments:
- velocity: float32 [3, 128, 64, 512], P(None, 'gx', 'gy', 'gz'), may hold values from -4 to 4
- sketch_prev: float32 [3, 64, 4, 32, 32, 128], P(None, 'gy', 'gz', 'gx'), may hold values from -6 to 6
- seed_matrix: int32 [512, 128], replicated, may hold values from -4 to 4
- snap_steps: int32 [4], replicated, may hold values from 0 to 511
- rank_keep: int32 [1], replicated, may hold values from 32 to 128
Outputs:
- velocity_out: float32 [3, 128, 64, 512], P(None, 'gx', 'gy', 'gz')
- mode_rows: float32 [3, 64, 4, 32, 32, 128], P(None, 'gy', 'gz', 'gx')
- factor: float32 [128, 128], replicated
The draws below stay inside these ranges and needn't reach their ends.
All inputs are finite; a program needn't handle non-finite values.
Results may differ from the reference program's by a relative error of at most 0.0003.
Values sent between devices are 32-bit elements; how exact they have to be, the bound alone decides.
No kernel may reach another device: no remote copies, remote signals or barrier semaphores. Data moves between devices by JAX's collectives and lax.ppermute only.
A program may use at most 64 MiB of HBM per device.

```python
import math
import jax
import jax.numpy as jnp
from jax import lax

SNAPS = 4
STEPS = 2
R = 128
MTOT = 512
NX = 128
NY = 64
NZ = 512
XC = 32
ZC = 128
ZCD = 32
NROWS = 786432
N_GZ = 4


def draw_sketch_prev(key, part):
    subkeys = jax.random.split(key, 4)
    full_shape = (3, NY, N_GZ, ZCD, XC, R)
    wall_frac = jnp.arange(NY, dtype=jnp.float32).reshape(1, NY, 1, 1, 1, 1) / max(NY - 1, 1)
    span_cells = jnp.arange(N_GZ, dtype=jnp.float32).reshape(1, 1, N_GZ, 1, 1, 1) * ZCD + jnp.arange(ZCD, dtype=jnp.float32).reshape(1, 1, 1, ZCD, 1, 1)
    span_frac = span_cells / max(N_GZ * ZCD - 1, 1)
    ramp_up = 1.0 + wall_frac + span_frac
    row_scale = jnp.exp(jax.random.uniform(subkeys[0], (3, NY, N_GZ, ZCD, XC, 1), jnp.float32) * math.log(10.0))
    noise = jax.random.truncated_normal(subkeys[1], -4.0, 4.0, full_shape, jnp.float32)
    col_scale = jnp.exp(jax.random.uniform(subkeys[3], (R,), jnp.float32) * math.log(10.0))
    return jnp.clip(0.02 * noise * row_scale * col_scale * ramp_up, -6.0, 6.0)


def plant(entries, rng, low, largest):
    longest = entries.shape.index(max(entries.shape))
    spots = []
    for shift in (0, 1):
        where = [jax.random.randint(jax.random.fold_in(rng, axis), (), 0, length) for axis, length in enumerate(entries.shape)]
        where[longest] = (where[longest] + shift) % entries.shape[longest]
        spots.append(tuple(where))
    return entries.at[spots[0]].set(low).at[spots[1]].set(largest)


def levels(rng, extent, shards, least, top_value):
    factor_of, own = 1.0, jax.random.fold_in(rng, 6)
    for position, parts in shards:
        heights = jnp.exp(jax.random.uniform(jax.random.fold_in(own, position), (parts,), jnp.float32, least / len(shards), top_value / len(shards)))
        factor_of = factor_of * jnp.repeat(heights, extent[position] // parts).reshape([-1 if axis == position else 1 for axis in range(len(extent))])
    return factor_of


def scatter_about(rng, dims, scale, most, pieces=(), kind=jnp.bfloat16):
    factor_of = levels(rng, dims, pieces, -0.22, 0.18) if pieces else 1.0
    values = jax.random.normal(rng, dims, jnp.float32) * scale * factor_of
    return jnp.minimum(jnp.maximum(values, -most), most).astype(kind)


def setup_inputs(seed: int = 0) -> dict:
    key_list = jax.random.split(jax.random.key(seed), 6)
    velocity = scatter_about(key_list[0], (3, NX, NY, NZ), 1.0, 4.0, ((1, 16), (2, 8), (3, 4)), jnp.float32)
    sketch_prev = draw_sketch_prev(jax.random.fold_in(key_list[5], 71), 0)
    seed_matrix = plant(jax.random.randint(key_list[2], (MTOT, R), -4, 5), jax.random.fold_in(key_list[2], 1), -4, 4).astype(jnp.int32)
    snap_steps = plant(jax.random.randint(key_list[3], (SNAPS,), 0, MTOT), jax.random.fold_in(key_list[3], 1), 0, MTOT - 1).astype(jnp.int32)
    rank_keep = jax.random.randint(key_list[4], (1,), R // 4, R + 1).astype(jnp.int32)
    return {"velocity": velocity, "sketch_prev": sketch_prev, "seed_matrix": seed_matrix, "snap_steps": snap_steps, "rank_keep": rank_keep}


TIME_STEP = 0.1
VISCOSITY = 0.4
ONE_THIRD = 1.0 / 3.0
TWO_THIRDS = 2.0 / 3.0
HIGHEST = lax.Precision.HIGHEST

def tendency(padded):
    center = padded[:, 1:-1, 1:-1, 1:-1]
    forward = (padded[:, 2:, 1:-1, 1:-1], padded[:, 1:-1, 2:, 1:-1], padded[:, 1:-1, 1:-1, 2:])
    backward = (padded[:, :-2, 1:-1, 1:-1], padded[:, 1:-1, :-2, 1:-1], padded[:, 1:-1, 1:-1, :-2])
    convect = center[0:1] * (forward[0] - backward[0]) + center[1:2] * (forward[1] - backward[1]) + center[2:3] * (forward[2] - backward[2])
    spread = forward[0] + backward[0] + forward[1] + backward[1] + forward[2] + backward[2] - 6.0 * center
    return -0.5 * convect + VISCOSITY * spread

def pad_walls(current):
    wrapped = jnp.pad(current, ((0, 0), (1, 1), (0, 0), (1, 1)), mode='wrap')
    return jnp.pad(wrapped, ((0, 0), (0, 0), (1, 1), (0, 0)))

def runge_step(current):
    first_section = current + TIME_STEP * tendency(pad_walls(current))
    second_section = 0.75 * current + 0.25 * (first_section + TIME_STEP * tendency(pad_walls(first_section)))
    return ONE_THIRD * current + TWO_THIRDS * (second_section + TIME_STEP * tendency(pad_walls(second_section)))

def reference(velocity, sketch_prev, seed_matrix, snap_steps, rank_keep):
    current = velocity
    snapshots = []
    for snap_index in range(SNAPS):
        for step_index in range(STEPS):
            current = runge_step(current)
        blocks = current.reshape(3, XC, 4, NY, ZC, 4)
        coarse = jnp.transpose(lax.optimization_barrier(jnp.mean(blocks, axis=(2, 5))), (0, 2, 3, 1))
        snapshots.append(coarse.reshape(-1))
    stacked = jnp.stack(snapshots)
    picker = (snap_steps[:, None] == jnp.arange(MTOT, dtype=jnp.int32)[None, :]).astype(jnp.float32)
    omega_rows = 0.5 * jnp.dot(picker, seed_matrix.astype(jnp.float32), precision=HIGHEST)
    sketch_rows = sketch_prev.reshape(-1, R) + lax.dot_general(stacked, omega_rows, (((0,), (0,)), ((), ())), precision=HIGHEST)
    gram_sum = lax.dot_general(sketch_rows, sketch_rows, (((0,), (0,)), ((), ())), precision=HIGHEST)
    lower_factor = jnp.linalg.cholesky(gram_sum)
    identity = jnp.eye(R, dtype=jnp.float32)
    inverse = lax.linalg.triangular_solve(lower_factor, identity, left_side=True, lower=True).T
    norm_scale = math.sqrt(NROWS)
    inside = (jnp.arange(R, dtype=jnp.int32) < rank_keep[0]).astype(jnp.float32)
    mode_rows = norm_scale * jnp.dot(sketch_rows, inverse, precision=HIGHEST) * inside[None, :]
    factor = lower_factor.T * (1.0 / norm_scale) * inside[:, None] * inside[None, :]
    return (current, mode_rows.reshape(3, NY, N_GZ, ZCD, XC, R), factor)
```

```python
import math

import jax
import jax.numpy as jnp
from jax import lax
from jax.sharding import PartitionSpec as P

SNAPS = 4
STEPS = 2
HALO = 3 * STEPS


TIME_STEP = 0.1
VISCOSITY = 0.4
ONE_THIRD = 1.0 / 3.0
TWO_THIRDS = 2.0 / 3.0
HIGHEST = lax.Precision.HIGHEST


def extended(block, sides, width):
    for axis, dim in sides:
        count = lax.axis_size(axis)
        forward = [(i, (i + 1) % count) for i in range(count)]
        backward = [(target, source) for source, target in forward]
        low = lax.ppermute(
            lax.slice_in_dim(block, block.shape[dim] - width, None, axis=dim), axis, forward
        )
        high = lax.ppermute(lax.slice_in_dim(block, 0, width, axis=dim), axis, backward)
        block = jnp.concatenate([low, block, high], axis=dim)
    return block


def tendency(padded):
    center = padded[:, 1:-1, 1:-1, 1:-1]
    forward = (padded[:, 2:, 1:-1, 1:-1], padded[:, 1:-1, 2:, 1:-1], padded[:, 1:-1, 1:-1, 2:])
    backward = (padded[:, :-2, 1:-1, 1:-1], padded[:, 1:-1, :-2, 1:-1], padded[:, 1:-1, 1:-1, :-2])
    convect = (
        center[0:1] * (forward[0] - backward[0])
        + center[1:2] * (forward[1] - backward[1])
        + center[2:3] * (forward[2] - backward[2])
    )
    spread = (
        forward[0]
        + backward[0]
        + forward[1]
        + backward[1]
        + forward[2]
        + backward[2]
        - 6.0 * center
    )
    return -0.5 * convect + VISCOSITY * spread


def trim(block, width):
    return block[:, width:-width, width:-width, width:-width]


def wall_mask(cells_y, margin):
    rows = lax.axis_index("gy") * cells_y - margin + jnp.arange(cells_y + 2 * margin, dtype=jnp.int32)
    inside = ((rows >= 0) & (rows < lax.axis_size("gy") * cells_y)).astype(jnp.float32)
    return inside[None, None, :, None]


def walled(block, cells_y, margin):
    if margin == 0:
        return block
    return block * wall_mask(cells_y, margin)


def step_shrinking(current, cells_y, margin):
    first_section = walled(trim(current, 1) + TIME_STEP * tendency(current), cells_y, margin - 1)
    second_section = walled(
        0.75 * trim(current, 2)
        + 0.25 * (trim(first_section, 1) + TIME_STEP * tendency(first_section)),
        cells_y,
        margin - 2,
    )
    return walled(
        ONE_THIRD * trim(current, 3)
        + TWO_THIRDS * (trim(second_section, 1) + TIME_STEP * tendency(second_section)),
        cells_y,
        margin - 3,
    )


def coarse_local(current):
    cells_x = current.shape[1]
    cells_y = current.shape[2]
    cells_z = current.shape[3]
    blocks = current.reshape(3, cells_x // 4, 4, cells_y, cells_z // 4, 4)
    return jnp.transpose(jnp.mean(blocks, axis=(2, 5)), (0, 2, 3, 1))


def butterfly_sum(value, axes):
    for axis in axes:
        count = lax.axis_size(axis)
        bit = 1
        while bit < count:
            value = value + lax.ppermute(value, axis, [(i, i ^ bit) for i in range(count)])
            bit *= 2
    return value


def on_device(velocity, sketch_prev, seed_matrix, snap_steps, rank_keep):
    current = velocity
    cells_y = current.shape[2]
    collected = []
    for snap_index in range(SNAPS):
        margin = HALO
        current = walled(extended(current, (("gx", 1), ("gy", 2), ("gz", 3)), HALO), cells_y, margin)
        for step_index in range(STEPS):
            current = step_shrinking(current, cells_y, margin)
            margin -= 3
        collected.append(coarse_local(current))
    stacked = lax.all_to_all(jnp.stack(collected), "gx", split_axis=3, concat_axis=4, tiled=True)
    rank_total = sketch_prev.shape[-1]
    snap_rows = stacked.reshape(stacked.shape[0], -1)
    picker = (
        snap_steps[:, None] == jnp.arange(seed_matrix.shape[0], dtype=jnp.int32)[None, :]
    ).astype(jnp.float32)
    omega_rows = 0.5 * jnp.dot(picker, seed_matrix.astype(jnp.float32), precision=HIGHEST)
    sketch_rows = sketch_prev.reshape(-1, rank_total) + lax.dot_general(
        snap_rows, omega_rows, (((0,), (0,)), ((), ())), precision=HIGHEST
    )
    local_gram = lax.dot_general(
        sketch_rows, sketch_rows, (((0,), (0,)), ((), ())), precision=HIGHEST
    )
    gram_sum = butterfly_sum(local_gram, ("gz", "gy", "gx"))
    lower_factor = jnp.linalg.cholesky(gram_sum)
    identity = jnp.eye(rank_total, dtype=jnp.float32)
    inverse = lax.linalg.triangular_solve(lower_factor, identity, left_side=True, lower=True).T
    total_rows = (
        sketch_rows.shape[0] * lax.axis_size("gx") * lax.axis_size("gy") * lax.axis_size("gz")
    )
    norm_scale = math.sqrt(total_rows)
    inside = (jnp.arange(rank_total, dtype=jnp.int32) < rank_keep[0]).astype(jnp.float32)
    mode_rows = norm_scale * jnp.dot(sketch_rows, inverse, precision=HIGHEST) * inside[None, :]
    factor = lower_factor.T * (1.0 / norm_scale) * inside[:, None] * inside[None, :]
    return (current, mode_rows.reshape(sketch_prev.shape), factor)


def solution(mesh):
    placed = (P(None, "gx", "gy", "gz"), P(None, "gy", "gz", "gx", None, None), P(), P(), P())
    return jax.shard_map(
        on_device,
        mesh=mesh,
        in_specs=placed,
        out_specs=(P(None, "gx", "gy", "gz"), P(None, "gy", "gz", "gx", None, None), P()),
        check_vma=False,
    )
```

```python
import math

import jax
import jax.numpy as jnp
from jax import lax
from jax.sharding import PartitionSpec as P

SNAPS = 4
STEPS = 2
HALO = 3 * STEPS


TIME_STEP = 0.1
VISCOSITY = 0.4
ONE_THIRD = 1.0 / 3.0
TWO_THIRDS = 2.0 / 3.0
HIGHEST = lax.Precision.HIGHEST


def extended(block, sides, width):
    for axis, dim in sides:
        count = lax.axis_size(axis)
        forward = [(i, (i + 1) % count) for i in range(count)]
        backward = [(target, source) for source, target in forward]
        low = lax.ppermute(
            lax.slice_in_dim(block, block.shape[dim] - width, None, axis=dim), axis, forward
        )
        high = lax.ppermute(lax.slice_in_dim(block, 0, width, axis=dim), axis, backward)
        block = jnp.concatenate([low, block, high], axis=dim)
    return block


def tendency(padded):
    center = padded[:, 1:-1, 1:-1, 1:-1]
    forward = (padded[:, 2:, 1:-1, 1:-1], padded[:, 1:-1, 2:, 1:-1], padded[:, 1:-1, 1:-1, 2:])
    backward = (padded[:, :-2, 1:-1, 1:-1], padded[:, 1:-1, :-2, 1:-1], padded[:, 1:-1, 1:-1, :-2])
    convect = (
        center[0:1] * (forward[0] - backward[0])
        + center[1:2] * (forward[1] - backward[1])
        + center[2:3] * (forward[2] - backward[2])
    )
    spread = (
        forward[0]
        + backward[0]
        + forward[1]
        + backward[1]
        + forward[2]
        + backward[2]
        - 6.0 * center
    )
    return -0.5 * convect + VISCOSITY * spread


def trim(block, width):
    return block[:, width:-width, width:-width, width:-width]


def wall_mask(cells_y, margin):
    rows = lax.axis_index("gy") * cells_y - margin + jnp.arange(cells_y + 2 * margin, dtype=jnp.int32)
    inside = ((rows >= 0) & (rows < lax.axis_size("gy") * cells_y)).astype(jnp.float32)
    return inside[None, None, :, None]


def walled(block, cells_y, margin):
    if margin == 0:
        return block
    return block * wall_mask(cells_y, margin)


def step_shrinking(current, cells_y, margin):
    first_section = walled(trim(current, 1) + TIME_STEP * tendency(current), cells_y, margin - 1)
    second_section = walled(
        0.75 * trim(current, 2)
        + 0.25 * (trim(first_section, 1) + TIME_STEP * tendency(first_section)),
        cells_y,
        margin - 2,
    )
    return walled(
        ONE_THIRD * trim(current, 3)
        + TWO_THIRDS * (trim(second_section, 1) + TIME_STEP * tendency(second_section)),
        cells_y,
        margin - 3,
    )


def coarse_local(current):
    cells_x = current.shape[1]
    cells_y = current.shape[2]
    cells_z = current.shape[3]
    blocks = current.reshape(3, cells_x // 4, 4, cells_y, cells_z // 4, 4)
    return jnp.transpose(jnp.mean(blocks, axis=(2, 5)), (0, 2, 3, 1))


def butterfly_sum(value, axes):
    for axis in axes:
        count = lax.axis_size(axis)
        bit = 1
        while bit < count:
            if 4 * bit <= count:
                near, far, both = (
                    lax.ppermute(value, axis, [(i, i ^ (shift * bit)) for i in range(count)])
                    for shift in (1, 2, 3)
                )
                value = (value + near) + (far + both)
                bit *= 4
            else:
                value = value + lax.ppermute(value, axis, [(i, i ^ bit) for i in range(count)])
                bit *= 2
    return value


def on_device(velocity, sketch_prev, seed_matrix, snap_steps, rank_keep):
    current = velocity
    cells_y = current.shape[2]
    collected = []
    for snap_index in range(SNAPS):
        margin = HALO
        current = walled(extended(current, (("gz", 3), ("gy", 2), ("gx", 1)), HALO), cells_y, margin)
        for step_index in range(STEPS):
            current = step_shrinking(current, cells_y, margin)
            margin -= 3
        collected.append(coarse_local(current))
    stacked = lax.all_to_all(jnp.stack(collected), "gx", split_axis=3, concat_axis=4, tiled=True)
    rank_total = sketch_prev.shape[-1]
    snap_rows = stacked.reshape(stacked.shape[0], -1)
    picker = (
        snap_steps[:, None] == jnp.arange(seed_matrix.shape[0], dtype=jnp.int32)[None, :]
    ).astype(jnp.float32)
    omega_rows = 0.5 * jnp.dot(picker, seed_matrix.astype(jnp.float32), precision=HIGHEST)
    sketch_rows = sketch_prev.reshape(-1, rank_total) + lax.dot_general(
        snap_rows, omega_rows, (((0,), (0,)), ((), ())), precision=HIGHEST
    )
    local_gram = lax.dot_general(
        sketch_rows, sketch_rows, (((0,), (0,)), ((), ())), precision=HIGHEST
    )
    gram_sum = butterfly_sum(local_gram, ("gz", "gy", "gx"))
    lower_factor = jnp.linalg.cholesky(gram_sum)
    identity = jnp.eye(rank_total, dtype=jnp.float32)
    inverse = lax.linalg.triangular_solve(lower_factor, identity, left_side=True, lower=True).T
    total_rows = (
        sketch_rows.shape[0] * lax.axis_size("gx") * lax.axis_size("gy") * lax.axis_size("gz")
    )
    norm_scale = math.sqrt(total_rows)
    inside = (jnp.arange(rank_total, dtype=jnp.int32) < rank_keep[0]).astype(jnp.float32)
    mode_rows = norm_scale * jnp.dot(sketch_rows, inverse, precision=HIGHEST) * inside[None, :]
    factor = lower_factor.T * (1.0 / norm_scale) * inside[:, None] * inside[None, :]
    return (current, mode_rows.reshape(sketch_prev.shape), factor)


def solution(mesh):
    placed = (P(None, "gx", "gy", "gz"), P(None, "gy", "gz", "gx", None, None), P(), P(), P())
    return jax.shard_map(
        on_device,
        mesh=mesh,
        in_specs=placed,
        out_specs=(P(None, "gx", "gy", "gz"), P(None, "gy", "gz", "gx", None, None), P()),
        check_vma=False,
    )
```

```python
import math

import jax
import jax.numpy as jnp
from jax import lax
from jax.sharding import PartitionSpec as P

SNAPS = 4
STEPS = 2
HALO = 3 * STEPS


TIME_STEP = 0.1
VISCOSITY = 0.4
ONE_THIRD = 1.0 / 3.0
TWO_THIRDS = 2.0 / 3.0
HIGHEST = lax.Precision.HIGHEST


def extended(block, sides, width):
    for axis, dim in sides:
        count = lax.axis_size(axis)
        forward = [(i, (i + 1) % count) for i in range(count)]
        backward = [(target, source) for source, target in forward]
        low = lax.ppermute(
            lax.slice_in_dim(block, block.shape[dim] - width, None, axis=dim), axis, forward
        )
        high = lax.ppermute(lax.slice_in_dim(block, 0, width, axis=dim), axis, backward)
        block = jnp.concatenate([low, block, high], axis=dim)
    return block


def tendency(padded):
    center = padded[:, 1:-1, 1:-1, 1:-1]
    forward = (padded[:, 2:, 1:-1, 1:-1], padded[:, 1:-1, 2:, 1:-1], padded[:, 1:-1, 1:-1, 2:])
    backward = (padded[:, :-2, 1:-1, 1:-1], padded[:, 1:-1, :-2, 1:-1], padded[:, 1:-1, 1:-1, :-2])
    convect = (
        center[0:1] * (forward[0] - backward[0])
        + center[1:2] * (forward[1] - backward[1])
        + center[2:3] * (forward[2] - backward[2])
    )
    spread = (
        forward[0]
        + backward[0]
        + forward[1]
        + backward[1]
        + forward[2]
        + backward[2]
        - 6.0 * center
    )
    return -0.5 * convect + VISCOSITY * spread


def trim(block, width):
    return block[:, width:-width, width:-width, width:-width]


def wall_mask(cells_y, margin):
    rows = lax.axis_index("gy") * cells_y - margin + jnp.arange(cells_y + 2 * margin, dtype=jnp.int32)
    inside = ((rows >= 0) & (rows < lax.axis_size("gy") * cells_y)).astype(jnp.float32)
    return inside[None, None, :, None]


def walled(block, cells_y, margin):
    if margin == 0:
        return block
    return block * wall_mask(cells_y, margin)


def step_shrinking(current, cells_y, margin):
    first_section = walled(trim(current, 1) + TIME_STEP * tendency(current), cells_y, margin - 1)
    second_section = walled(
        0.75 * trim(current, 2)
        + 0.25 * (trim(first_section, 1) + TIME_STEP * tendency(first_section)),
        cells_y,
        margin - 2,
    )
    return walled(
        ONE_THIRD * trim(current, 3)
        + TWO_THIRDS * (trim(second_section, 1) + TIME_STEP * tendency(second_section)),
        cells_y,
        margin - 3,
    )


def coarse_local(current):
    cells_x = current.shape[1]
    cells_y = current.shape[2]
    cells_z = current.shape[3]
    blocks = current.reshape(3, cells_x // 4, 4, cells_y, cells_z // 4, 4)
    return jnp.transpose(jnp.mean(blocks, axis=(2, 5)), (0, 2, 3, 1))


def butterfly_sum(value, axes):
    for axis in axes:
        count = lax.axis_size(axis)
        bit = 1
        while bit < count:
            if 4 * bit <= count:
                near, far, both = (
                    lax.ppermute(value, axis, [(i, i ^ (shift * bit)) for i in range(count)])
                    for shift in (1, 2, 3)
                )
                value = (value + near) + (far + both)
                bit *= 4
            else:
                value = value + lax.ppermute(value, axis, [(i, i ^ bit) for i in range(count)])
                bit *= 2
    return value


def on_device(velocity, sketch_prev, seed_matrix, snap_steps, rank_keep):
    solver_prev = lax.all_to_all(sketch_prev, "gx", split_axis=4, concat_axis=3, tiled=True)
    current = velocity
    cells_y = current.shape[2]
    collected = []
    for snap_index in range(SNAPS):
        margin = HALO
        current = walled(extended(current, (("gz", 3), ("gy", 2), ("gx", 1)), HALO), cells_y, margin)
        for step_index in range(STEPS):
            current = step_shrinking(current, cells_y, margin)
            margin -= 3
        collected.append(coarse_local(current))
    rank_total = sketch_prev.shape[-1]
    picker = (
        snap_steps[:, None] == jnp.arange(seed_matrix.shape[0], dtype=jnp.int32)[None, :]
    ).astype(jnp.float32)
    omega_rows = 0.5 * jnp.dot(picker, seed_matrix.astype(jnp.float32), precision=HIGHEST)
    local_snaps = jnp.stack(collected)
    solver_rows = solver_prev.reshape(-1, rank_total) + lax.dot_general(
        local_snaps.reshape(local_snaps.shape[0], -1), omega_rows, (((0,), (0,)), ((), ())),
        precision=HIGHEST,
    )
    local_gram = lax.dot_general(
        solver_rows, solver_rows, (((0,), (0,)), ((), ())), precision=HIGHEST
    )
    gram_sum = butterfly_sum(local_gram, ("gz", "gy", "gx"))
    stacked = lax.all_to_all(local_snaps, "gx", split_axis=3, concat_axis=4, tiled=True)
    snap_rows = stacked.reshape(stacked.shape[0], -1)
    sketch_rows = sketch_prev.reshape(-1, rank_total) + lax.dot_general(
        snap_rows, omega_rows, (((0,), (0,)), ((), ())), precision=HIGHEST
    )
    lower_factor = jnp.linalg.cholesky(gram_sum)
    identity = jnp.eye(rank_total, dtype=jnp.float32)
    inverse = lax.linalg.triangular_solve(lower_factor, identity, left_side=True, lower=True).T
    total_rows = (
        sketch_rows.shape[0] * lax.axis_size("gx") * lax.axis_size("gy") * lax.axis_size("gz")
    )
    norm_scale = math.sqrt(total_rows)
    inside = (jnp.arange(rank_total, dtype=jnp.int32) < rank_keep[0]).astype(jnp.float32)
    mode_rows = norm_scale * jnp.dot(sketch_rows, inverse, precision=HIGHEST) * inside[None, :]
    factor = lower_factor.T * (1.0 / norm_scale) * inside[:, None] * inside[None, :]
    return (current, mode_rows.reshape(sketch_prev.shape), factor)


def solution(mesh):
    placed = (P(None, "gx", "gy", "gz"), P(None, "gy", "gz", "gx", None, None), P(), P(), P())
    return jax.shard_map(
        on_device,
        mesh=mesh,
        in_specs=placed,
        out_specs=(P(None, "gx", "gy", "gz"), P(None, "gy", "gz", "gx", None, None), P()),
        check_vma=False,
    )
```

```python
import math

import jax
import jax.numpy as jnp
from jax import lax
from jax.sharding import PartitionSpec as P

SNAPS = 4
STEPS = 2
HALO = 3 * STEPS


TIME_STEP = 0.1
VISCOSITY = 0.4
ONE_THIRD = 1.0 / 3.0
TWO_THIRDS = 2.0 / 3.0
HIGHEST = lax.Precision.HIGHEST


def extended(block, sides, width):
    for axis, dim in sides:
        count = lax.axis_size(axis)
        forward = [(i, (i + 1) % count) for i in range(count)]
        backward = [(target, source) for source, target in forward]
        low = lax.ppermute(
            lax.slice_in_dim(block, block.shape[dim] - width, None, axis=dim), axis, forward
        )
        high = lax.ppermute(lax.slice_in_dim(block, 0, width, axis=dim), axis, backward)
        block = jnp.concatenate([low, block, high], axis=dim)
    return block


def tendency(padded):
    center = padded[:, 1:-1, 1:-1, 1:-1]
    forward = (padded[:, 2:, 1:-1, 1:-1], padded[:, 1:-1, 2:, 1:-1], padded[:, 1:-1, 1:-1, 2:])
    backward = (padded[:, :-2, 1:-1, 1:-1], padded[:, 1:-1, :-2, 1:-1], padded[:, 1:-1, 1:-1, :-2])
    convect = (
        center[0:1] * (forward[0] - backward[0])
        + center[1:2] * (forward[1] - backward[1])
        + center[2:3] * (forward[2] - backward[2])
    )
    spread = (
        forward[0]
        + backward[0]
        + forward[1]
        + backward[1]
        + forward[2]
        + backward[2]
        - 6.0 * center
    )
    return -0.5 * convect + VISCOSITY * spread


def trim(block, width):
    return block[:, width:-width, width:-width, width:-width]


def wall_mask(cells_y, margin):
    rows = lax.axis_index("gy") * cells_y - margin + jnp.arange(cells_y + 2 * margin, dtype=jnp.int32)
    inside = ((rows >= 0) & (rows < lax.axis_size("gy") * cells_y)).astype(jnp.float32)
    return inside[None, None, :, None]


def walled(block, cells_y, margin):
    if margin == 0:
        return block
    return block * wall_mask(cells_y, margin)


def step_shrinking(current, cells_y, margin):
    first_section = walled(trim(current, 1) + TIME_STEP * tendency(current), cells_y, margin - 1)
    second_section = walled(
        0.75 * trim(current, 2)
        + 0.25 * (trim(first_section, 1) + TIME_STEP * tendency(first_section)),
        cells_y,
        margin - 2,
    )
    return walled(
        ONE_THIRD * trim(current, 3)
        + TWO_THIRDS * (trim(second_section, 1) + TIME_STEP * tendency(second_section)),
        cells_y,
        margin - 3,
    )


def coarse_local(current):
    cells_x = current.shape[1]
    cells_y = current.shape[2]
    cells_z = current.shape[3]
    blocks = current.reshape(3, cells_x // 4, 4, cells_y, cells_z // 4, 4)
    return jnp.transpose(jnp.mean(blocks, axis=(2, 5)), (0, 2, 3, 1))


def butterfly_sum(value, axes):
    for axis in axes:
        count = lax.axis_size(axis)
        bit = 1
        while bit < count:
            if 4 * bit <= count:
                near, far, both = (
                    lax.ppermute(value, axis, [(i, i ^ (shift * bit)) for i in range(count)])
                    for shift in (1, 2, 3)
                )
                value = (value + near) + (far + both)
                bit *= 4
            else:
                value = value + lax.ppermute(value, axis, [(i, i ^ bit) for i in range(count)])
                bit *= 2
    return value


def on_device(velocity, sketch_prev, seed_matrix, snap_steps, rank_keep):
    current = velocity
    cells_y = current.shape[2]

    def snapshot_round(snap_index, carry):
        current, collected = carry
        margin = HALO
        current = walled(extended(current, (("gz", 3), ("gy", 2), ("gx", 1)), HALO), cells_y, margin)
        for step_index in range(STEPS):
            current = step_shrinking(current, cells_y, margin)
            margin -= 3
        collected = lax.dynamic_update_index_in_dim(collected, coarse_local(current), snap_index, 0)
        return current, collected

    collected = jnp.zeros((SNAPS,) + coarse_local(current).shape, current.dtype)
    current, collected = lax.fori_loop(0, SNAPS, snapshot_round, (current, collected))
    stacked = lax.all_to_all(collected, "gx", split_axis=3, concat_axis=4, tiled=True)
    rank_total = sketch_prev.shape[-1]
    snap_rows = stacked.reshape(stacked.shape[0], -1)
    picker = (
        snap_steps[:, None] == jnp.arange(seed_matrix.shape[0], dtype=jnp.int32)[None, :]
    ).astype(jnp.float32)
    omega_rows = 0.5 * jnp.dot(picker, seed_matrix.astype(jnp.float32), precision=HIGHEST)
    sketch_rows = sketch_prev.reshape(-1, rank_total) + lax.dot_general(
        snap_rows, omega_rows, (((0,), (0,)), ((), ())), precision=HIGHEST
    )
    local_gram = lax.dot_general(
        sketch_rows, sketch_rows, (((0,), (0,)), ((), ())), precision=HIGHEST
    )
    gram_sum = butterfly_sum(local_gram, ("gz", "gy", "gx"))
    lower_factor = jnp.linalg.cholesky(gram_sum)
    identity = jnp.eye(rank_total, dtype=jnp.float32)
    inverse = lax.linalg.triangular_solve(lower_factor, identity, left_side=True, lower=True).T
    total_rows = (
        sketch_rows.shape[0] * lax.axis_size("gx") * lax.axis_size("gy") * lax.axis_size("gz")
    )
    norm_scale = math.sqrt(total_rows)
    inside = (jnp.arange(rank_total, dtype=jnp.int32) < rank_keep[0]).astype(jnp.float32)
    mode_rows = norm_scale * jnp.dot(sketch_rows, inverse, precision=HIGHEST) * inside[None, :]
    factor = lower_factor.T * (1.0 / norm_scale) * inside[:, None] * inside[None, :]
    return (current, mode_rows.reshape(sketch_prev.shape), factor)


def solution(mesh):
    placed = (P(None, "gx", "gy", "gz"), P(None, "gy", "gz", "gx", None, None), P(), P(), P())
    return jax.shard_map(
        on_device,
        mesh=mesh,
        in_specs=placed,
        out_specs=(P(None, "gx", "gy", "gz"), P(None, "gy", "gz", "gx", None, None), P()),
        check_vma=False,
    )
```

```python
import math

import jax
import jax.numpy as jnp
from jax import lax
from jax.sharding import PartitionSpec as P

SNAPS = 4
STEPS = 2
HALO = 3 * STEPS


TIME_STEP = 0.1
VISCOSITY = 0.4
ONE_THIRD = 1.0 / 3.0
TWO_THIRDS = 2.0 / 3.0
HIGHEST = lax.Precision.HIGHEST


def extended(block, sides, width):
    for axis, dim in sides:
        count = lax.axis_size(axis)
        forward = [(i, (i + 1) % count) for i in range(count)]
        backward = [(target, source) for source, target in forward]
        low = lax.ppermute(
            lax.slice_in_dim(block, block.shape[dim] - width, None, axis=dim), axis, forward
        )
        high = lax.ppermute(lax.slice_in_dim(block, 0, width, axis=dim), axis, backward)
        block = jnp.concatenate([low, block, high], axis=dim)
    return block


def tendency(padded):
    center = padded[:, 1:-1, 1:-1, 1:-1]
    forward = (padded[:, 2:, 1:-1, 1:-1], padded[:, 1:-1, 2:, 1:-1], padded[:, 1:-1, 1:-1, 2:])
    backward = (padded[:, :-2, 1:-1, 1:-1], padded[:, 1:-1, :-2, 1:-1], padded[:, 1:-1, 1:-1, :-2])
    convect = (
        center[0:1] * (forward[0] - backward[0])
        + center[1:2] * (forward[1] - backward[1])
        + center[2:3] * (forward[2] - backward[2])
    )
    spread = (
        forward[0]
        + backward[0]
        + forward[1]
        + backward[1]
        + forward[2]
        + backward[2]
        - 6.0 * center
    )
    return -0.5 * convect + VISCOSITY * spread


def trim(block, width):
    return block[:, width:-width, width:-width, width:-width]


def wall_mask(cells_y, margin):
    rows = lax.axis_index("gy") * cells_y - margin + jnp.arange(cells_y + 2 * margin, dtype=jnp.int32)
    inside = ((rows >= 0) & (rows < lax.axis_size("gy") * cells_y)).astype(jnp.float32)
    return inside[None, None, :, None]


def walled(block, cells_y, margin):
    if margin == 0:
        return block
    return block * wall_mask(cells_y, margin)


def step_shrinking(current, cells_y, margin):
    first_section = walled(trim(current, 1) + TIME_STEP * tendency(current), cells_y, margin - 1)
    second_section = walled(
        0.75 * trim(current, 2)
        + 0.25 * (trim(first_section, 1) + TIME_STEP * tendency(first_section)),
        cells_y,
        margin - 2,
    )
    return walled(
        ONE_THIRD * trim(current, 3)
        + TWO_THIRDS * (trim(second_section, 1) + TIME_STEP * tendency(second_section)),
        cells_y,
        margin - 3,
    )


def coarse_local(current):
    cells_x = current.shape[1]
    cells_y = current.shape[2]
    cells_z = current.shape[3]
    blocks = current.reshape(3, cells_x // 4, 4, cells_y, cells_z // 4, 4)
    return jnp.mean(blocks, axis=(2, 5))


def butterfly_sum(value, axes):
    for axis in axes:
        count = lax.axis_size(axis)
        bit = 1
        while bit < count:
            if 4 * bit <= count:
                near, far, both = (
                    lax.ppermute(value, axis, [(i, i ^ (shift * bit)) for i in range(count)])
                    for shift in (1, 2, 3)
                )
                value = (value + near) + (far + both)
                bit *= 4
            else:
                value = value + lax.ppermute(value, axis, [(i, i ^ bit) for i in range(count)])
                bit *= 2
    return value


def on_device(velocity, sketch_prev, seed_matrix, snap_steps, rank_keep):
    current = velocity
    cells_y = current.shape[2]

    def snapshot_round(snap_index, carry):
        current, collected = carry
        margin = HALO
        current = walled(extended(current, (("gz", 3), ("gy", 2), ("gx", 1)), HALO), cells_y, margin)
        for step_index in range(STEPS):
            current = step_shrinking(current, cells_y, margin)
            margin -= 3
        collected = lax.dynamic_update_index_in_dim(collected, coarse_local(current), snap_index, 0)
        return current, collected

    collected = jnp.zeros((SNAPS,) + coarse_local(current).shape, current.dtype)
    current, collected = lax.fori_loop(0, SNAPS, snapshot_round, (current, collected))
    collected = jnp.transpose(collected, (0, 1, 3, 4, 2))
    stacked = lax.all_to_all(collected, "gx", split_axis=3, concat_axis=4, tiled=True)
    rank_total = sketch_prev.shape[-1]
    snap_rows = stacked.reshape(stacked.shape[0], -1)
    picker = (
        snap_steps[:, None] == jnp.arange(seed_matrix.shape[0], dtype=jnp.int32)[None, :]
    ).astype(jnp.float32)
    omega_rows = 0.5 * jnp.dot(picker, seed_matrix.astype(jnp.float32), precision=HIGHEST)
    sketch_rows = sketch_prev.reshape(-1, rank_total) + lax.dot_general(
        snap_rows, omega_rows, (((0,), (0,)), ((), ())), precision=HIGHEST
    )
    local_gram = lax.dot_general(
        sketch_rows, sketch_rows, (((0,), (0,)), ((), ())), precision=HIGHEST
    )
    gram_sum = butterfly_sum(local_gram, ("gz", "gy", "gx"))
    lower_factor = jnp.linalg.cholesky(gram_sum)
    identity = jnp.eye(rank_total, dtype=jnp.float32)
    inverse = lax.linalg.triangular_solve(lower_factor, identity, left_side=True, lower=True).T
    total_rows = (
        sketch_rows.shape[0] * lax.axis_size("gx") * lax.axis_size("gy") * lax.axis_size("gz")
    )
    norm_scale = math.sqrt(total_rows)
    inside = (jnp.arange(rank_total, dtype=jnp.int32) < rank_keep[0]).astype(jnp.float32)
    mode_rows = norm_scale * jnp.dot(sketch_rows, inverse, precision=HIGHEST) * inside[None, :]
    factor = lower_factor.T * (1.0 / norm_scale) * inside[:, None] * inside[None, :]
    return (current, mode_rows.reshape(sketch_prev.shape), factor)


def solution(mesh):
    placed = (P(None, "gx", "gy", "gz"), P(None, "gy", "gz", "gx", None, None), P(), P(), P())
    return jax.shard_map(
        on_device,
        mesh=mesh,
        in_specs=placed,
        out_specs=(P(None, "gx", "gy", "gz"), P(None, "gy", "gz", "gx", None, None), P()),
        check_vma=False,
    )
```

```python
import math

import jax
import jax.numpy as jnp
from jax import lax
from jax.sharding import PartitionSpec as P

SNAPS = 4
STEPS = 2
HALO = 3 * STEPS


TIME_STEP = 0.1
VISCOSITY = 0.4
ONE_THIRD = 1.0 / 3.0
TWO_THIRDS = 2.0 / 3.0
HIGHEST = lax.Precision.HIGHEST


def extended(block, sides, width):
    for axis, dim in sides:
        count = lax.axis_size(axis)
        forward = [(i, (i + 1) % count) for i in range(count)]
        backward = [(target, source) for source, target in forward]
        low = lax.ppermute(
            lax.slice_in_dim(block, block.shape[dim] - width, None, axis=dim), axis, forward
        )
        high = lax.ppermute(lax.slice_in_dim(block, 0, width, axis=dim), axis, backward)
        block = jnp.concatenate([low, block, high], axis=dim)
    return block


def tendency(padded):
    center = padded[:, 1:-1, 1:-1, 1:-1]
    forward = (padded[:, 2:, 1:-1, 1:-1], padded[:, 1:-1, 2:, 1:-1], padded[:, 1:-1, 1:-1, 2:])
    backward = (padded[:, :-2, 1:-1, 1:-1], padded[:, 1:-1, :-2, 1:-1], padded[:, 1:-1, 1:-1, :-2])
    convect = (
        center[0:1] * (forward[0] - backward[0])
        + center[1:2] * (forward[1] - backward[1])
        + center[2:3] * (forward[2] - backward[2])
    )
    spread = (
        forward[0]
        + backward[0]
        + forward[1]
        + backward[1]
        + forward[2]
        + backward[2]
        - 6.0 * center
    )
    return -0.5 * convect + VISCOSITY * spread


def trim(block, width):
    return block[:, width:-width, width:-width, width:-width]


def wall_mask(cells_y, margin):
    rows = lax.axis_index("gy") * cells_y - margin + jnp.arange(cells_y + 2 * margin, dtype=jnp.int32)
    inside = ((rows >= 0) & (rows < lax.axis_size("gy") * cells_y)).astype(jnp.float32)
    return inside[None, None, :, None]


def walled(block, cells_y, margin):
    if margin == 0:
        return block
    return block * wall_mask(cells_y, margin)


def step_shrinking(current, cells_y, margin):
    first_section = walled(trim(current, 1) + TIME_STEP * tendency(current), cells_y, margin - 1)
    second_section = walled(
        0.75 * trim(current, 2)
        + 0.25 * (trim(first_section, 1) + TIME_STEP * tendency(first_section)),
        cells_y,
        margin - 2,
    )
    return walled(
        ONE_THIRD * trim(current, 3)
        + TWO_THIRDS * (trim(second_section, 1) + TIME_STEP * tendency(second_section)),
        cells_y,
        margin - 3,
    )


def coarse_local(current):
    cells_x = current.shape[1]
    cells_y = current.shape[2]
    cells_z = current.shape[3]
    blocks = current.reshape(3, cells_x // 4, 4, cells_y, cells_z // 4, 4)
    return jnp.mean(blocks, axis=(2, 5))


def butterfly_sum(value, axes):
    for axis in axes:
        count = lax.axis_size(axis)
        bit = 1
        while bit < count:
            if bit == 1 and 4 <= count:
                near, far, both = (
                    lax.ppermute(value, axis, [(i, i ^ (shift * bit)) for i in range(count)])
                    for shift in (1, 2, 3)
                )
                value = (value + near) + (far + both)
                bit *= 4
            else:
                value = value + lax.ppermute(value, axis, [(i, i ^ bit) for i in range(count)])
                bit *= 2
    return value


def on_device(velocity, sketch_prev, seed_matrix, snap_steps, rank_keep):
    current = velocity
    cells_y = current.shape[2]

    def snapshot_round(snap_index, carry):
        current, collected = carry
        margin = HALO
        current = walled(extended(current, (("gz", 3), ("gy", 2), ("gx", 1)), HALO), cells_y, margin)
        for step_index in range(STEPS):
            current = step_shrinking(current, cells_y, margin)
            margin -= 3
        collected = lax.dynamic_update_index_in_dim(collected, coarse_local(current), snap_index, 0)
        return current, collected

    collected = jnp.zeros((SNAPS,) + coarse_local(current).shape, current.dtype)
    current, collected = lax.fori_loop(0, SNAPS, snapshot_round, (current, collected))
    collected = jnp.transpose(collected, (0, 1, 3, 4, 2))
    stacked = lax.all_to_all(collected, "gx", split_axis=3, concat_axis=4, tiled=True)
    rank_total = sketch_prev.shape[-1]
    snap_rows = stacked.reshape(stacked.shape[0], -1)
    picker = (
        snap_steps[:, None] == jnp.arange(seed_matrix.shape[0], dtype=jnp.int32)[None, :]
    ).astype(jnp.float32)
    omega_rows = 0.5 * jnp.dot(picker, seed_matrix.astype(jnp.float32), precision=HIGHEST)
    sketch_rows = sketch_prev.reshape(-1, rank_total) + lax.dot_general(
        snap_rows, omega_rows, (((0,), (0,)), ((), ())), precision=HIGHEST
    )
    local_gram = lax.dot_general(
        sketch_rows, sketch_rows, (((0,), (0,)), ((), ())), precision=HIGHEST
    )
    gram_sum = butterfly_sum(local_gram, ("gz", "gy", "gx"))
    lower_factor = jnp.linalg.cholesky(gram_sum)
    identity = jnp.eye(rank_total, dtype=jnp.float32)
    inverse = lax.linalg.triangular_solve(lower_factor, identity, left_side=True, lower=True).T
    total_rows = (
        sketch_rows.shape[0] * lax.axis_size("gx") * lax.axis_size("gy") * lax.axis_size("gz")
    )
    norm_scale = math.sqrt(total_rows)
    inside = (jnp.arange(rank_total, dtype=jnp.int32) < rank_keep[0]).astype(jnp.float32)
    mode_rows = norm_scale * jnp.dot(sketch_rows, inverse, precision=HIGHEST) * inside[None, :]
    factor = lower_factor.T * (1.0 / norm_scale) * inside[:, None] * inside[None, :]
    return (current, mode_rows.reshape(sketch_prev.shape), factor)


def solution(mesh):
    placed = (P(None, "gx", "gy", "gz"), P(None, "gy", "gz", "gx", None, None), P(), P(), P())
    return jax.shard_map(
        on_device,
        mesh=mesh,
        in_specs=placed,
        out_specs=(P(None, "gx", "gy", "gz"), P(None, "gy", "gz", "gx", None, None), P()),
        check_vma=False,
    )
```

```python
import math

import jax
import jax.numpy as jnp
from jax import lax
from jax.sharding import PartitionSpec as P

SNAPS = 4
STEPS = 2
HALO = 3 * STEPS


TIME_STEP = 0.1
VISCOSITY = 0.4
ONE_THIRD = 1.0 / 3.0
TWO_THIRDS = 2.0 / 3.0
HIGHEST = lax.Precision.HIGHEST


def extended(block, sides, width):
    for axis, dim in sides:
        count = lax.axis_size(axis)
        forward = [(i, (i + 1) % count) for i in range(count)]
        backward = [(target, source) for source, target in forward]
        low = lax.ppermute(
            lax.slice_in_dim(block, block.shape[dim] - width, None, axis=dim), axis, forward
        )
        high = lax.ppermute(lax.slice_in_dim(block, 0, width, axis=dim), axis, backward)
        block = jnp.concatenate([low, block, high], axis=dim)
    return block


def tendency(padded):
    center = padded[:, 1:-1, 1:-1, 1:-1]
    forward = (padded[:, 2:, 1:-1, 1:-1], padded[:, 1:-1, 2:, 1:-1], padded[:, 1:-1, 1:-1, 2:])
    backward = (padded[:, :-2, 1:-1, 1:-1], padded[:, 1:-1, :-2, 1:-1], padded[:, 1:-1, 1:-1, :-2])
    convect = (
        center[0:1] * (forward[0] - backward[0])
        + center[1:2] * (forward[1] - backward[1])
        + center[2:3] * (forward[2] - backward[2])
    )
    spread = (
        forward[0]
        + backward[0]
        + forward[1]
        + backward[1]
        + forward[2]
        + backward[2]
        - 6.0 * center
    )
    return -0.5 * convect + VISCOSITY * spread


def trim(block, width):
    return block[:, width:-width, width:-width, width:-width]


def wall_mask(cells_y, margin):
    rows = lax.axis_index("gy") * cells_y - margin + jnp.arange(cells_y + 2 * margin, dtype=jnp.int32)
    inside = ((rows >= 0) & (rows < lax.axis_size("gy") * cells_y)).astype(jnp.float32)
    return inside[None, None, :, None]


def walled(block, cells_y, margin):
    if margin == 0:
        return block
    return block * wall_mask(cells_y, margin)


def step_shrinking(current, cells_y, margin):
    first_section = walled(trim(current, 1) + TIME_STEP * tendency(current), cells_y, margin - 1)
    second_section = walled(
        0.75 * trim(current, 2)
        + 0.25 * (trim(first_section, 1) + TIME_STEP * tendency(first_section)),
        cells_y,
        margin - 2,
    )
    return walled(
        ONE_THIRD * trim(current, 3)
        + TWO_THIRDS * (trim(second_section, 1) + TIME_STEP * tendency(second_section)),
        cells_y,
        margin - 3,
    )


def coarse_local(current):
    cells_x = current.shape[1]
    cells_y = current.shape[2]
    cells_z = current.shape[3]
    blocks = current.reshape(3, cells_x // 4, 4, cells_y, cells_z // 4, 4)
    return jnp.mean(blocks, axis=(2, 5))


def butterfly_sum(value, axes):
    for axis in axes:
        count = lax.axis_size(axis)
        bit = 1
        while bit < count:
            if 4 * bit <= count:
                near, far, both = (
                    lax.ppermute(value, axis, [(i, i ^ (shift * bit)) for i in range(count)])
                    for shift in (1, 2, 3)
                )
                value = (value + near) + (far + both)
                bit *= 4
            else:
                value = value + lax.ppermute(value, axis, [(i, i ^ bit) for i in range(count)])
                bit *= 2
    return value


def on_device(velocity, sketch_prev, seed_matrix, snap_steps, rank_keep):
    cells_y = velocity.shape[2]
    cells_z = velocity.shape[3]
    span_halo = HALO * SNAPS
    current = extended(velocity, (("gz", 3),), span_halo)

    def snapshot_round(snap_index, carry):
        current, collected = carry
        margin = HALO
        current = walled(extended(current, (("gy", 2), ("gx", 1)), HALO), cells_y, margin)
        for step_index in range(STEPS):
            current = step_shrinking(current, cells_y, margin)
            margin -= 3
        own = current[..., span_halo - HALO : span_halo - HALO + cells_z]
        collected = lax.dynamic_update_index_in_dim(collected, coarse_local(own), snap_index, 0)
        current = jnp.pad(current, ((0, 0), (0, 0), (0, 0), (HALO, HALO)))
        return current, collected

    collected = jnp.zeros((SNAPS,) + coarse_local(velocity).shape, velocity.dtype)
    current, collected = lax.fori_loop(0, SNAPS, snapshot_round, (current, collected))
    current = current[..., span_halo : span_halo + cells_z]
    collected = jnp.transpose(collected, (0, 1, 3, 4, 2))
    stacked = lax.all_to_all(collected, "gx", split_axis=3, concat_axis=4, tiled=True)
    rank_total = sketch_prev.shape[-1]
    snap_rows = stacked.reshape(stacked.shape[0], -1)
    picker = (
        snap_steps[:, None] == jnp.arange(seed_matrix.shape[0], dtype=jnp.int32)[None, :]
    ).astype(jnp.float32)
    omega_rows = 0.5 * jnp.dot(picker, seed_matrix.astype(jnp.float32), precision=HIGHEST)
    sketch_rows = sketch_prev.reshape(-1, rank_total) + lax.dot_general(
        snap_rows, omega_rows, (((0,), (0,)), ((), ())), precision=HIGHEST
    )
    local_gram = lax.dot_general(
        sketch_rows, sketch_rows, (((0,), (0,)), ((), ())), precision=HIGHEST
    )
    gram_sum = butterfly_sum(local_gram, ("gz", "gy", "gx"))
    lower_factor = jnp.linalg.cholesky(gram_sum)
    identity = jnp.eye(rank_total, dtype=jnp.float32)
    inverse = lax.linalg.triangular_solve(lower_factor, identity, left_side=True, lower=True).T
    total_rows = (
        sketch_rows.shape[0] * lax.axis_size("gx") * lax.axis_size("gy") * lax.axis_size("gz")
    )
    norm_scale = math.sqrt(total_rows)
    inside = (jnp.arange(rank_total, dtype=jnp.int32) < rank_keep[0]).astype(jnp.float32)
    mode_rows = norm_scale * jnp.dot(sketch_rows, inverse, precision=HIGHEST) * inside[None, :]
    factor = lower_factor.T * (1.0 / norm_scale) * inside[:, None] * inside[None, :]
    return (current, mode_rows.reshape(sketch_prev.shape), factor)


def solution(mesh):
    placed = (P(None, "gx", "gy", "gz"), P(None, "gy", "gz", "gx", None, None), P(), P(), P())
    return jax.shard_map(
        on_device,
        mesh=mesh,
        in_specs=placed,
        out_specs=(P(None, "gx", "gy", "gz"), P(None, "gy", "gz", "gx", None, None), P()),
        check_vma=False,
    )
```

```python
import math

import jax
import jax.numpy as jnp
from jax import lax
from jax.sharding import PartitionSpec as P

SNAPS = 4
STEPS = 2
HALO = 3 * STEPS


TIME_STEP = 0.1
VISCOSITY = 0.4
ONE_THIRD = 1.0 / 3.0
TWO_THIRDS = 2.0 / 3.0
HIGHEST = lax.Precision.HIGHEST


def extended(block, sides, width):
    for axis, dim in sides:
        count = lax.axis_size(axis)
        forward = [(i, (i + 1) % count) for i in range(count)]
        backward = [(target, source) for source, target in forward]
        low = lax.ppermute(
            lax.slice_in_dim(block, block.shape[dim] - width, None, axis=dim), axis, forward
        )
        high = lax.ppermute(lax.slice_in_dim(block, 0, width, axis=dim), axis, backward)
        block = jnp.concatenate([low, block, high], axis=dim)
    return block


def tendency(padded):
    center = padded[:, 1:-1, 1:-1, 1:-1]
    forward = (padded[:, 2:, 1:-1, 1:-1], padded[:, 1:-1, 2:, 1:-1], padded[:, 1:-1, 1:-1, 2:])
    backward = (padded[:, :-2, 1:-1, 1:-1], padded[:, 1:-1, :-2, 1:-1], padded[:, 1:-1, 1:-1, :-2])
    convect = (
        center[0:1] * (forward[0] - backward[0])
        + center[1:2] * (forward[1] - backward[1])
        + center[2:3] * (forward[2] - backward[2])
    )
    spread = (
        forward[0]
        + backward[0]
        + forward[1]
        + backward[1]
        + forward[2]
        + backward[2]
        - 6.0 * center
    )
    return -0.5 * convect + VISCOSITY * spread


def trim(block, width):
    return block[:, width:-width, width:-width, width:-width]


def wall_mask(cells_y, margin):
    rows = lax.axis_index("gy") * cells_y - margin + jnp.arange(cells_y + 2 * margin, dtype=jnp.int32)
    inside = ((rows >= 0) & (rows < lax.axis_size("gy") * cells_y)).astype(jnp.float32)
    return inside[None, None, :, None]


def walled(block, cells_y, margin):
    if margin == 0:
        return block
    return block * wall_mask(cells_y, margin)


def step_shrinking(current, cells_y, margin):
    first_section = walled(trim(current, 1) + TIME_STEP * tendency(current), cells_y, margin - 1)
    second_section = walled(
        0.75 * trim(current, 2)
        + 0.25 * (trim(first_section, 1) + TIME_STEP * tendency(first_section)),
        cells_y,
        margin - 2,
    )
    return walled(
        ONE_THIRD * trim(current, 3)
        + TWO_THIRDS * (trim(second_section, 1) + TIME_STEP * tendency(second_section)),
        cells_y,
        margin - 3,
    )


def coarse_local(current):
    cells_x = current.shape[1]
    cells_y = current.shape[2]
    cells_z = current.shape[3]
    blocks = current.reshape(3, cells_x // 4, 4, cells_y, cells_z // 4, 4)
    return jnp.mean(blocks, axis=(2, 5))


def butterfly_sum(value, axes):
    for axis in axes:
        count = lax.axis_size(axis)
        bit = 1
        while bit < count:
            if 4 * bit <= count:
                near, far, both = (
                    lax.ppermute(value, axis, [(i, i ^ (shift * bit)) for i in range(count)])
                    for shift in (1, 2, 3)
                )
                value = (value + near) + (far + both)
                bit *= 4
            else:
                value = value + lax.ppermute(value, axis, [(i, i ^ bit) for i in range(count)])
                bit *= 2
    return value


def pack_symmetric(gram):
    half = gram.shape[0] // 2
    top, bottom = gram[:half, :half], gram[half:, half:]
    lower = jnp.tril(jnp.ones((half, half), jnp.bool_))
    blocks = jnp.concatenate([gram[half:, :half], jnp.where(lower, top, bottom)], axis=1)
    corner = jnp.concatenate([jnp.diagonal(bottom), jnp.zeros((half,), gram.dtype)])
    return jnp.concatenate([blocks, corner[None, :]], axis=0)


def unpack_symmetric(packed):
    half = packed.shape[0] - 1
    side, both = packed[:half, :half], packed[:half, half:]
    top = jnp.tril(both) + jnp.tril(both, -1).T
    bottom = jnp.triu(both, 1) + jnp.triu(both, 1).T + jnp.diag(packed[half, :half])
    return jnp.concatenate(
        [jnp.concatenate([top, side.T], axis=1), jnp.concatenate([side, bottom], axis=1)], axis=0
    )


def on_device(velocity, sketch_prev, seed_matrix, snap_steps, rank_keep):
    cells_y = velocity.shape[2]
    cells_z = velocity.shape[3]
    span_halo = HALO * SNAPS
    current = extended(velocity, (("gz", 3),), span_halo)

    def snapshot_round(snap_index, carry):
        current, collected = carry
        margin = HALO
        current = walled(extended(current, (("gy", 2), ("gx", 1)), HALO), cells_y, margin)
        for step_index in range(STEPS):
            current = step_shrinking(current, cells_y, margin)
            margin -= 3
        own = current[..., span_halo - HALO : span_halo - HALO + cells_z]
        collected = lax.dynamic_update_index_in_dim(collected, coarse_local(own), snap_index, 0)
        current = jnp.pad(current, ((0, 0), (0, 0), (0, 0), (HALO, HALO)))
        return current, collected

    collected = jnp.zeros((SNAPS,) + coarse_local(velocity).shape, velocity.dtype)
    current, collected = lax.fori_loop(0, SNAPS, snapshot_round, (current, collected))
    current = current[..., span_halo : span_halo + cells_z]
    collected = jnp.transpose(collected, (0, 1, 3, 4, 2))
    stacked = lax.all_to_all(collected, "gx", split_axis=3, concat_axis=4, tiled=True)
    rank_total = sketch_prev.shape[-1]
    snap_rows = stacked.reshape(stacked.shape[0], -1)
    picker = (
        snap_steps[:, None] == jnp.arange(seed_matrix.shape[0], dtype=jnp.int32)[None, :]
    ).astype(jnp.float32)
    omega_rows = 0.5 * jnp.dot(picker, seed_matrix.astype(jnp.float32), precision=HIGHEST)
    sketch_rows = sketch_prev.reshape(-1, rank_total) + lax.dot_general(
        snap_rows, omega_rows, (((0,), (0,)), ((), ())), precision=HIGHEST
    )
    local_gram = lax.dot_general(
        sketch_rows, sketch_rows, (((0,), (0,)), ((), ())), precision=HIGHEST
    )
    gram_sum = unpack_symmetric(butterfly_sum(pack_symmetric(local_gram), ("gz", "gy", "gx")))
    lower_factor = jnp.linalg.cholesky(gram_sum)
    identity = jnp.eye(rank_total, dtype=jnp.float32)
    inverse = lax.linalg.triangular_solve(lower_factor, identity, left_side=True, lower=True).T
    total_rows = (
        sketch_rows.shape[0] * lax.axis_size("gx") * lax.axis_size("gy") * lax.axis_size("gz")
    )
    norm_scale = math.sqrt(total_rows)
    inside = (jnp.arange(rank_total, dtype=jnp.int32) < rank_keep[0]).astype(jnp.float32)
    mode_rows = norm_scale * jnp.dot(sketch_rows, inverse, precision=HIGHEST) * inside[None, :]
    factor = lower_factor.T * (1.0 / norm_scale) * inside[:, None] * inside[None, :]
    return (current, mode_rows.reshape(sketch_prev.shape), factor)


def solution(mesh):
    placed = (P(None, "gx", "gy", "gz"), P(None, "gy", "gz", "gx", None, None), P(), P(), P())
    return jax.shard_map(
        on_device,
        mesh=mesh,
        in_specs=placed,
        out_specs=(P(None, "gx", "gy", "gz"), P(None, "gy", "gz", "gx", None, None), P()),
        check_vma=False,
    )
```

```python
import math

import jax
import jax.numpy as jnp
from jax import lax
from jax.sharding import PartitionSpec as P

SNAPS = 4
STEPS = 2
HALO = 3 * STEPS


TIME_STEP = 0.1
VISCOSITY = 0.4
ONE_THIRD = 1.0 / 3.0
TWO_THIRDS = 2.0 / 3.0
HIGHEST = lax.Precision.HIGHEST


def extended(block, sides, width, walled_axis=None):
    for axis, dim in sides:
        count = lax.axis_size(axis)
        forward = [(i, (i + 1) % count) for i in range(count - (axis == walled_axis))]
        backward = [(target, source) for source, target in forward]
        low = lax.ppermute(
            lax.slice_in_dim(block, block.shape[dim] - width, None, axis=dim), axis, forward
        )
        high = lax.ppermute(lax.slice_in_dim(block, 0, width, axis=dim), axis, backward)
        block = jnp.concatenate([low, block, high], axis=dim)
    return block


def tendency(padded):
    center = padded[:, 1:-1, 1:-1, 1:-1]
    forward = (padded[:, 2:, 1:-1, 1:-1], padded[:, 1:-1, 2:, 1:-1], padded[:, 1:-1, 1:-1, 2:])
    backward = (padded[:, :-2, 1:-1, 1:-1], padded[:, 1:-1, :-2, 1:-1], padded[:, 1:-1, 1:-1, :-2])
    convect = (
        center[0:1] * (forward[0] - backward[0])
        + center[1:2] * (forward[1] - backward[1])
        + center[2:3] * (forward[2] - backward[2])
    )
    spread = (
        forward[0]
        + backward[0]
        + forward[1]
        + backward[1]
        + forward[2]
        + backward[2]
        - 6.0 * center
    )
    return -0.5 * convect + VISCOSITY * spread


def trim(block, width):
    return block[:, width:-width, width:-width, width:-width]


def wall_mask(cells_y, margin):
    rows = lax.axis_index("gy") * cells_y - margin + jnp.arange(cells_y + 2 * margin, dtype=jnp.int32)
    inside = ((rows >= 0) & (rows < lax.axis_size("gy") * cells_y)).astype(jnp.float32)
    return inside[None, None, :, None]


def walled(block, cells_y, margin):
    if margin == 0:
        return block
    return block * wall_mask(cells_y, margin)


def step_shrinking(current, cells_y, margin):
    first_section = walled(trim(current, 1) + TIME_STEP * tendency(current), cells_y, margin - 1)
    second_section = walled(
        0.75 * trim(current, 2)
        + 0.25 * (trim(first_section, 1) + TIME_STEP * tendency(first_section)),
        cells_y,
        margin - 2,
    )
    return walled(
        ONE_THIRD * trim(current, 3)
        + TWO_THIRDS * (trim(second_section, 1) + TIME_STEP * tendency(second_section)),
        cells_y,
        margin - 3,
    )


def coarse_local(current):
    cells_x = current.shape[1]
    cells_y = current.shape[2]
    cells_z = current.shape[3]
    blocks = current.reshape(3, cells_x // 4, 4, cells_y, cells_z // 4, 4)
    return jnp.mean(blocks, axis=(2, 5))


def butterfly_sum(value, axes):
    for axis in axes:
        count = lax.axis_size(axis)
        bit = 1
        while bit < count:
            if 4 * bit <= count:
                near, far, both = (
                    lax.ppermute(value, axis, [(i, i ^ (shift * bit)) for i in range(count)])
                    for shift in (1, 2, 3)
                )
                value = (value + near) + (far + both)
                bit *= 4
            else:
                value = value + lax.ppermute(value, axis, [(i, i ^ bit) for i in range(count)])
                bit *= 2
    return value


def on_device(velocity, sketch_prev, seed_matrix, snap_steps, rank_keep):
    cells_y = velocity.shape[2]
    cells_z = velocity.shape[3]
    span_halo = HALO * SNAPS
    current = extended(velocity, (("gz", 3),), span_halo)

    def snapshot_round(snap_index, carry):
        current, collected = carry
        margin = HALO
        current = extended(current, (("gy", 2), ("gx", 1)), HALO, walled_axis="gy")
        for step_index in range(STEPS):
            current = step_shrinking(current, cells_y, margin)
            margin -= 3
        own = current[..., span_halo - HALO : span_halo - HALO + cells_z]
        collected = lax.dynamic_update_index_in_dim(collected, coarse_local(own), snap_index, 0)
        current = jnp.pad(current, ((0, 0), (0, 0), (0, 0), (HALO, HALO)))
        return current, collected

    collected = jnp.zeros((SNAPS,) + coarse_local(velocity).shape, velocity.dtype)
    current, collected = lax.fori_loop(0, SNAPS, snapshot_round, (current, collected))
    current = current[..., span_halo : span_halo + cells_z]
    collected = jnp.transpose(collected, (0, 1, 3, 4, 2))
    stacked = lax.all_to_all(collected, "gx", split_axis=3, concat_axis=4, tiled=True)
    rank_total = sketch_prev.shape[-1]
    snap_rows = stacked.reshape(stacked.shape[0], -1)
    picker = (
        snap_steps[:, None] == jnp.arange(seed_matrix.shape[0], dtype=jnp.int32)[None, :]
    ).astype(jnp.float32)
    omega_rows = 0.5 * jnp.dot(picker, seed_matrix.astype(jnp.float32), precision=HIGHEST)
    sketch_rows = sketch_prev.reshape(-1, rank_total) + lax.dot_general(
        snap_rows, omega_rows, (((0,), (0,)), ((), ())), precision=HIGHEST
    )
    local_gram = lax.dot_general(
        sketch_rows, sketch_rows, (((0,), (0,)), ((), ())), precision=HIGHEST
    )
    gram_sum = butterfly_sum(local_gram, ("gz", "gy", "gx"))
    lower_factor = jnp.linalg.cholesky(gram_sum)
    identity = jnp.eye(rank_total, dtype=jnp.float32)
    inverse = lax.linalg.triangular_solve(lower_factor, identity, left_side=True, lower=True).T
    total_rows = (
        sketch_rows.shape[0] * lax.axis_size("gx") * lax.axis_size("gy") * lax.axis_size("gz")
    )
    norm_scale = math.sqrt(total_rows)
    inside = (jnp.arange(rank_total, dtype=jnp.int32) < rank_keep[0]).astype(jnp.float32)
    mode_rows = norm_scale * jnp.dot(sketch_rows, inverse, precision=HIGHEST) * inside[None, :]
    factor = lower_factor.T * (1.0 / norm_scale) * inside[:, None] * inside[None, :]
    return (current, mode_rows.reshape(sketch_prev.shape), factor)


def solution(mesh):
    placed = (P(None, "gx", "gy", "gz"), P(None, "gy", "gz", "gx", None, None), P(), P(), P())
    return jax.shard_map(
        on_device,
        mesh=mesh,
        in_specs=placed,
        out_specs=(P(None, "gx", "gy", "gz"), P(None, "gy", "gz", "gx", None, None), P()),
        check_vma=False,
    )
```

```python
import math

import jax
import jax.numpy as jnp
from jax import lax
from jax.sharding import PartitionSpec as P

SNAPS = 4
STEPS = 2
HALO = 3 * STEPS


TIME_STEP = 0.1
VISCOSITY = 0.4
ONE_THIRD = 1.0 / 3.0
TWO_THIRDS = 2.0 / 3.0
HIGHEST = lax.Precision.HIGHEST


def extended(block, sides, width, walled_axis=None):
    for axis, dim in sides:
        count = lax.axis_size(axis)
        forward = [(i, (i + 1) % count) for i in range(count - (axis == walled_axis))]
        backward = [(target, source) for source, target in forward]
        low = lax.ppermute(
            lax.slice_in_dim(block, block.shape[dim] - width, None, axis=dim), axis, forward
        )
        high = lax.ppermute(lax.slice_in_dim(block, 0, width, axis=dim), axis, backward)
        block = jnp.concatenate([low, block, high], axis=dim)
    return block


def tendency(padded):
    center = padded[:, 1:-1, 1:-1, 1:-1]
    forward = (padded[:, 2:, 1:-1, 1:-1], padded[:, 1:-1, 2:, 1:-1], padded[:, 1:-1, 1:-1, 2:])
    backward = (padded[:, :-2, 1:-1, 1:-1], padded[:, 1:-1, :-2, 1:-1], padded[:, 1:-1, 1:-1, :-2])
    convect = (
        center[0:1] * (forward[0] - backward[0])
        + center[1:2] * (forward[1] - backward[1])
        + center[2:3] * (forward[2] - backward[2])
    )
    spread = (
        forward[0]
        + backward[0]
        + forward[1]
        + backward[1]
        + forward[2]
        + backward[2]
        - 6.0 * center
    )
    return -0.5 * convect + VISCOSITY * spread


def trim(block, width):
    return block[:, width:-width, width:-width, width:-width]


def wall_mask(cells_y, margin):
    rows = lax.axis_index("gy") * cells_y - margin + jnp.arange(cells_y + 2 * margin, dtype=jnp.int32)
    inside = ((rows >= 0) & (rows < lax.axis_size("gy") * cells_y)).astype(jnp.float32)
    return inside[None, None, :, None]


def walled(block, cells_y, margin):
    if margin == 0:
        return block
    return block * wall_mask(cells_y, margin)


def step_shrinking(current, cells_y, margin):
    first_section = walled(trim(current, 1) + TIME_STEP * tendency(current), cells_y, margin - 1)
    second_section = walled(
        0.75 * trim(current, 2)
        + 0.25 * (trim(first_section, 1) + TIME_STEP * tendency(first_section)),
        cells_y,
        margin - 2,
    )
    return walled(
        ONE_THIRD * trim(current, 3)
        + TWO_THIRDS * (trim(second_section, 1) + TIME_STEP * tendency(second_section)),
        cells_y,
        margin - 3,
    )


def coarse_local(current):
    cells_x = current.shape[1]
    cells_y = current.shape[2]
    cells_z = current.shape[3]
    blocks = current.reshape(3, cells_x // 4, 4, cells_y, cells_z // 4, 4)
    return jnp.mean(blocks, axis=(2, 5))


def butterfly_sum(value, axes):
    for axis in axes:
        count = lax.axis_size(axis)
        bit = 1
        while bit < count:
            if 4 * bit <= count:
                near, far, both = (
                    lax.ppermute(value, axis, [(i, i ^ (shift * bit)) for i in range(count)])
                    for shift in (1, 2, 3)
                )
                value = (value + near) + (far + both)
                bit *= 4
            else:
                value = value + lax.ppermute(value, axis, [(i, i ^ bit) for i in range(count)])
                bit *= 2
    return value


def on_device(velocity, sketch_prev, seed_matrix, snap_steps, rank_keep):
    cells_y = velocity.shape[2]
    cells_z = velocity.shape[3]
    span_halo = HALO * SNAPS
    current = extended(velocity, (("gz", 3),), span_halo)

    def snapshot_round(snap_index, carry):
        current, collected = carry
        margin = HALO
        current = extended(current, (("gx", 1), ("gy", 2)), HALO, walled_axis="gy")
        for step_index in range(STEPS):
            current = step_shrinking(current, cells_y, margin)
            margin -= 3
        own = current[..., span_halo - HALO : span_halo - HALO + cells_z]
        collected = lax.dynamic_update_index_in_dim(collected, coarse_local(own), snap_index, 0)
        current = jnp.pad(current, ((0, 0), (0, 0), (0, 0), (HALO, HALO)))
        return current, collected

    collected = jnp.zeros((SNAPS,) + coarse_local(velocity).shape, velocity.dtype)
    current, collected = lax.fori_loop(0, SNAPS, snapshot_round, (current, collected))
    current = current[..., span_halo : span_halo + cells_z]
    collected = jnp.transpose(collected, (0, 1, 3, 4, 2))
    stacked = lax.all_to_all(collected, "gx", split_axis=3, concat_axis=4, tiled=True)
    rank_total = sketch_prev.shape[-1]
    snap_rows = stacked.reshape(stacked.shape[0], -1)
    picker = (
        snap_steps[:, None] == jnp.arange(seed_matrix.shape[0], dtype=jnp.int32)[None, :]
    ).astype(jnp.float32)
    omega_rows = 0.5 * jnp.dot(picker, seed_matrix.astype(jnp.float32), precision=HIGHEST)
    sketch_rows = sketch_prev.reshape(-1, rank_total) + lax.dot_general(
        snap_rows, omega_rows, (((0,), (0,)), ((), ())), precision=HIGHEST
    )
    local_gram = lax.dot_general(
        sketch_rows, sketch_rows, (((0,), (0,)), ((), ())), precision=HIGHEST
    )
    gram_sum = butterfly_sum(local_gram, ("gz", "gy", "gx"))
    lower_factor = jnp.linalg.cholesky(gram_sum)
    identity = jnp.eye(rank_total, dtype=jnp.float32)
    inverse = lax.linalg.triangular_solve(lower_factor, identity, left_side=True, lower=True).T
    total_rows = (
        sketch_rows.shape[0] * lax.axis_size("gx") * lax.axis_size("gy") * lax.axis_size("gz")
    )
    norm_scale = math.sqrt(total_rows)
    inside = (jnp.arange(rank_total, dtype=jnp.int32) < rank_keep[0]).astype(jnp.float32)
    mode_rows = norm_scale * jnp.dot(sketch_rows, inverse, precision=HIGHEST) * inside[None, :]
    factor = lower_factor.T * (1.0 / norm_scale) * inside[:, None] * inside[None, :]
    return (current, mode_rows.reshape(sketch_prev.shape), factor)


def solution(mesh):
    placed = (P(None, "gx", "gy", "gz"), P(None, "gy", "gz", "gx", None, None), P(), P(), P())
    return jax.shard_map(
        on_device,
        mesh=mesh,
        in_specs=placed,
        out_specs=(P(None, "gx", "gy", "gz"), P(None, "gy", "gz", "gx", None, None), P()),
        check_vma=False,
    )
```

```python
import math

import jax
import jax.numpy as jnp
from jax import lax
from jax.sharding import PartitionSpec as P

SNAPS = 4
STEPS = 2
HALO = 3 * STEPS


TIME_STEP = 0.1
VISCOSITY = 0.4
ONE_THIRD = 1.0 / 3.0
TWO_THIRDS = 2.0 / 3.0
HIGHEST = lax.Precision.HIGHEST


def extended(block, sides, width, walled_axis=None):
    for axis, dim in sides:
        count = lax.axis_size(axis)
        forward = [(i, (i + 1) % count) for i in range(count - (axis == walled_axis))]
        backward = [(target, source) for source, target in forward]
        low = lax.ppermute(
            lax.slice_in_dim(block, block.shape[dim] - width, None, axis=dim), axis, forward
        )
        high = lax.ppermute(lax.slice_in_dim(block, 0, width, axis=dim), axis, backward)
        block = jnp.concatenate([low, block, high], axis=dim)
    return block


def tendency(padded):
    center = padded[:, 1:-1, 1:-1, 1:-1]
    forward = (padded[:, 2:, 1:-1, 1:-1], padded[:, 1:-1, 2:, 1:-1], padded[:, 1:-1, 1:-1, 2:])
    backward = (padded[:, :-2, 1:-1, 1:-1], padded[:, 1:-1, :-2, 1:-1], padded[:, 1:-1, 1:-1, :-2])
    convect = (
        center[0:1] * (forward[0] - backward[0])
        + center[1:2] * (forward[1] - backward[1])
        + center[2:3] * (forward[2] - backward[2])
    )
    spread = (
        forward[0]
        + backward[0]
        + forward[1]
        + backward[1]
        + forward[2]
        + backward[2]
        - 6.0 * center
    )
    return -0.5 * convect + VISCOSITY * spread


def trim(block, width):
    return block[:, width:-width, width:-width, width:-width]


def wall_mask(cells_y, margin):
    rows = lax.axis_index("gy") * cells_y - margin + jnp.arange(cells_y + 2 * margin, dtype=jnp.int32)
    inside = ((rows >= 0) & (rows < lax.axis_size("gy") * cells_y)).astype(jnp.float32)
    return inside[None, None, :, None]


def walled(block, cells_y, margin):
    if margin == 0:
        return block
    return block * wall_mask(cells_y, margin)


def step_shrinking(current, cells_y, margin):
    first_section = walled(trim(current, 1) + TIME_STEP * tendency(current), cells_y, margin - 1)
    second_section = walled(
        0.75 * trim(current, 2)
        + 0.25 * (trim(first_section, 1) + TIME_STEP * tendency(first_section)),
        cells_y,
        margin - 2,
    )
    return walled(
        ONE_THIRD * trim(current, 3)
        + TWO_THIRDS * (trim(second_section, 1) + TIME_STEP * tendency(second_section)),
        cells_y,
        margin - 3,
    )


def coarse_local(current):
    cells_x = current.shape[1]
    cells_y = current.shape[2]
    cells_z = current.shape[3]
    blocks = current.reshape(3, cells_x // 4, 4, cells_y, cells_z // 4, 4)
    return jnp.mean(blocks, axis=(2, 5))


def butterfly_sum(value, axes):
    for axis in axes:
        count = lax.axis_size(axis)
        bit = 1
        while bit < count:
            if 4 * bit <= count:
                near, far, both = (
                    lax.ppermute(value, axis, [(i, i ^ (shift * bit)) for i in range(count)])
                    for shift in (1, 2, 3)
                )
                value = (value + near) + (far + both)
                bit *= 4
            else:
                value = value + lax.ppermute(value, axis, [(i, i ^ bit) for i in range(count)])
                bit *= 2
    return value


def on_device(velocity, sketch_prev, seed_matrix, snap_steps, rank_keep):
    cells_y = velocity.shape[2]
    cells_z = velocity.shape[3]
    span_halo = HALO * SNAPS
    current = extended(velocity, (("gz", 3),), span_halo)

    def snapshot_round(snap_index, carry):
        current, collected = carry
        margin = HALO
        current = extended(current, (("gy", 2), ("gx", 1)), HALO, walled_axis="gy")
        for step_index in range(STEPS):
            current = step_shrinking(current, cells_y, margin)
            margin -= 3
        own = current[..., span_halo - HALO : span_halo - HALO + cells_z]
        collected = lax.dynamic_update_index_in_dim(collected, coarse_local(own), snap_index, 0)
        current = jnp.pad(current, ((0, 0), (0, 0), (0, 0), (HALO, HALO)))
        return current, collected

    collected = jnp.zeros((SNAPS,) + coarse_local(velocity).shape, velocity.dtype)
    current, collected = lax.fori_loop(0, SNAPS, snapshot_round, (current, collected))
    current = current[..., span_halo : span_halo + cells_z]
    collected = jnp.transpose(collected, (0, 1, 3, 4, 2))
    stacked = lax.all_to_all(collected, "gx", split_axis=3, concat_axis=4, tiled=True)
    rank_total = sketch_prev.shape[-1]
    snap_rows = stacked.reshape(stacked.shape[0], -1)
    picker = (
        snap_steps[:, None] == jnp.arange(seed_matrix.shape[0], dtype=jnp.int32)[None, :]
    ).astype(jnp.float32)
    omega_rows = 0.5 * jnp.dot(picker, seed_matrix.astype(jnp.float32), precision=HIGHEST)
    sketch_rows = sketch_prev.reshape(-1, rank_total) + lax.dot_general(
        snap_rows, omega_rows, (((0,), (0,)), ((), ())), precision=HIGHEST
    )
    local_gram = lax.dot_general(
        sketch_rows, sketch_rows, (((0,), (0,)), ((), ())), precision=HIGHEST
    )
    gram_sum = butterfly_sum(local_gram, ("gz", "gy", "gx"))
    lower_factor = lax.linalg.cholesky(0.5 * (gram_sum + gram_sum.T), symmetrize_input=False)
    identity = jnp.eye(rank_total, dtype=jnp.float32)
    inverse = lax.linalg.triangular_solve(
        lower_factor, identity, left_side=False, lower=True, transpose_a=True
    )
    total_rows = (
        sketch_rows.shape[0] * lax.axis_size("gx") * lax.axis_size("gy") * lax.axis_size("gz")
    )
    norm_scale = math.sqrt(total_rows)
    inside = (jnp.arange(rank_total, dtype=jnp.int32) < rank_keep[0]).astype(jnp.float32)
    mode_rows = norm_scale * jnp.dot(sketch_rows, inverse, precision=HIGHEST) * inside[None, :]
    factor = lower_factor.T * (1.0 / norm_scale) * inside[:, None] * inside[None, :]
    return (current, mode_rows.reshape(sketch_prev.shape), factor)


def solution(mesh):
    placed = (P(None, "gx", "gy", "gz"), P(None, "gy", "gz", "gx", None, None), P(), P(), P())
    return jax.shard_map(
        on_device,
        mesh=mesh,
        in_specs=placed,
        out_specs=(P(None, "gx", "gy", "gz"), P(None, "gy", "gz", "gx", None, None), P()),
        check_vma=False,
    )
```
